256 devices in a mesh: gx: 16 (over y, x_hi, core), gy: 16 (over z, x_lo).
Axes of the slice: x: 4 (x_hi: 2, x_lo: 2; x = x_hi * 2 + x_lo), y: 4, z: 8, core: 2. Of those that a mesh axis runs over, the one named last changes fastest.
Arguments:
- features: bfloat16 [16, 16, 2, 512, 128], P('gx', 'gy'), may hold values from -6 to 6
- occupancy: int32 [16, 16, 2, 512], P('gx', 'gy'), may hold values 0 or 1
- brick_pos: int32 [16, 16, 2], P('gx', 'gy'), may hold values from 0 to 15, as said below
- brick_count: int32 [16, 16], P('gx', 'gy'), may hold values from 1 to 2, as said below
- weight: bfloat16 [27, 128, 128], replicated, may hold values from -0.109375 to 0.109375
- cotangent: bfloat16 [16, 16, 2, 512, 128], P('gx', 'gy'), may hold values from -6 to 6
Outputs:
- output: bfloat16 [16, 16, 2, 512, 128], P('gx', 'gy')
- input_grad: bfloat16 [16, 16, 2, 512, 128], P('gx', 'gy')
- weight_grad: float32 [27, 128, 128], replicated
The draws below stay inside these ranges and needn't reach their ends.
Inputs may be any that keep to these rules, and one draw needn't show every extreme that they name: `brick_pos`: within a tile the 2 slots hold distinct positions. `brick_count`: some tile holds exactly 2 live slots.
All inputs are finite; a program needn't handle non-finite values. No bound on the sum of `occupancy` on one device may be relied on, other than what follows from the above.
Results may differ from the reference program's by a relative error of at most 0.001.
Values may be sent and summed in bfloat16 or wider, within the bound.
No kernel may reach another device: no remote copies, remote signals or barrier semaphores. Data moves between devices by JAX's collectives and lax.ppermute only.
A program may use at most 64 MiB of HBM per device.

```python
import jax
import jax.numpy as jnp
from jax import lax

C = 128
BRICK = 8
VOX = 512
TBX = 2
TBY = 2
ZL = 4
NB = 2
OFFS = 27
TILES_X = 16
TILES_Y = 16


def draw_brick_pos(key, part):
    keys = jax.random.split(key, TILES_X * TILES_Y)
    orders = jax.vmap(lambda single: jax.random.permutation(single, TBX * TBY * ZL))(keys)
    return orders[:, :NB].reshape(TILES_X, TILES_Y, NB).astype(jnp.int32)


def draw_brick_count(key, part):
    tiles = TILES_X * TILES_Y
    raw = jax.random.randint(key, (tiles,), 1, NB + 1)
    counts = jnp.maximum(1, raw * raw // NB)
    fullest = jax.random.randint(jax.random.fold_in(key, 7), (), 0, tiles)
    counts = jnp.where(jnp.arange(tiles) == fullest, NB, counts)
    return counts.reshape(TILES_X, TILES_Y).astype(jnp.int32)


def touch_ends(array, key, least, largest):
    longest = array.shape.index(max(array.shape))
    spots = []
    for shift in (0, 1):
        where = [jax.random.randint(jax.random.fold_in(key, axis), (), 0, length) for axis, length in enumerate(array.shape)]
        where[longest] = (where[longest] + shift) % array.shape[longest]
        spots.append(tuple(where))
    return array.at[spots[0]].set(least).at[spots[1]].set(largest)


def block_levels(stream_key, dims, cuts, low, top_value):
    def one(axis_at, shards_of):
        draws = jax.random.uniform(jax.random.fold_in(jax.random.fold_in(stream_key, 6), axis_at), (shards_of,), jnp.float32, low / len(cuts), top_value / len(cuts))
        return jnp.repeat(jnp.exp(draws), dims[axis_at] // shards_of).reshape((-1,) + (1,) * (len(dims) - axis_at - 1))

    loudness = one(*cuts[0])
    for cut in cuts[1:]:
        loudness = loudness * one(*cut)
    return loudness


def normal_values(stream_key, shape, width, most, cuts=(), kind=jnp.bfloat16):
    array = jax.random.normal(stream_key, shape, jnp.float32) * width
    if len(cuts) > 0:
        array = block_levels(stream_key, shape, cuts, -0.22, 0.18) * array
    return jnp.clip(array, min=-most, max=most).astype(kind)


def setup_inputs(seed: int = 0) -> dict:
    seeds = jax.random.split(jax.random.key(seed), 7)
    return {
        "features": normal_values(seeds[0], (TILES_X, TILES_Y, NB, VOX, C), 1.0, 6.0, ((0, 16), (1, 16))),
        "occupancy": touch_ends((jax.random.randint(seeds[1], (TILES_X, TILES_Y, NB, VOX), 0, 2) < 1).astype(jnp.int32), jax.random.fold_in(seeds[1], 1), 0, 1),
        "brick_pos": draw_brick_pos(jax.random.fold_in(seeds[6], 71), 0),
        "brick_count": draw_brick_count(jax.random.fold_in(seeds[6], 71), 0),
        "weight": normal_values(seeds[4], (OFFS, C, C), (OFFS * C) ** -0.5, 0.109375),
        "cotangent": normal_values(seeds[5], (TILES_X, TILES_Y, NB, VOX, C), 1.0, 6.0, ((0, 16), (1, 16))),
    }


def place_bricks(bricks, places, alive):
    spots = jnp.arange(TBX * TBY * ZL, dtype=jnp.int32)
    picker = ((places[None, :] == spots[:, None]) & alive[None, :]).astype(jnp.float32)
    dense = jnp.einsum("ps,svc->pvc", picker, bricks.astype(jnp.float32)).astype(jnp.bfloat16)
    dense = dense.reshape(TBX, TBY, ZL, BRICK, BRICK, BRICK, C)
    dense = dense.transpose(0, 3, 1, 4, 2, 5, 6)
    return dense.reshape(TBX * BRICK, TBY * BRICK, ZL * BRICK, C)


def cut_windows(padded, places):
    along_x = (places // (TBY * ZL)).astype(jnp.int32)
    along_y = ((places // ZL) % TBY).astype(jnp.int32)
    along_z = (places % ZL).astype(jnp.int32)
    zero_index = jnp.zeros_like(along_x)

    def one_window(start_x, start_y, start_z, start_c):
        return lax.dynamic_slice(padded, (start_x, start_y, start_z, start_c), (BRICK + 2, BRICK + 2, BRICK + 2, C))

    return jax.vmap(one_window)(along_x * BRICK, along_y * BRICK, along_z * BRICK, zero_index)


def offset_rows(windows, offset):
    first = offset // 9
    second = (offset // 3) % 3
    third = offset % 3
    piece = windows[:, first:first + BRICK, second:second + BRICK, third:third + BRICK, :]
    return piece.reshape(-1, C)


def to_global(dense):
    dense = dense.reshape(TILES_X, TILES_Y, TBX * BRICK, TBY * BRICK, ZL * BRICK, C)
    dense = dense.transpose(0, 2, 1, 3, 4, 5)
    dense = dense.reshape(TILES_X * TBX * BRICK, TILES_Y * TBY * BRICK, ZL * BRICK, C)
    return jnp.pad(dense, ((1, 1), (1, 1), (1, 1), (0, 0)))


def reference(features, occupancy, brick_pos, brick_count, weight, cotangent):
    tiles = TILES_X * TILES_Y
    places = brick_pos.reshape(tiles, NB).astype(jnp.int32)
    alive_all = jnp.arange(NB, dtype=jnp.int32)[None, :] < brick_count.reshape(tiles, 1)
    keeper = (occupancy.reshape(tiles, NB, VOX) * alive_all[:, :, None].astype(jnp.int32)).astype(jnp.bfloat16)
    feat_masked = features.reshape(tiles, NB, VOX, C) * keeper[..., None]
    grad_masked = cotangent.reshape(tiles, NB, VOX, C) * keeper[..., None]

    def build(items):
        return place_bricks(items[0], items[1], items[2])

    feat_global = to_global(lax.map(build, (feat_masked, places, alive_all)))
    grad_global = to_global(lax.map(build, (grad_masked, places, alive_all)))
    zero_index = jnp.zeros((), jnp.int32)
    extent = (TBX * BRICK + 2, TBY * BRICK + 2, ZL * BRICK + 2, C)

    def tile_step(total, index):
        row = (index // TILES_Y).astype(jnp.int32)
        column = (index % TILES_Y).astype(jnp.int32)
        starts = (row * (TBX * BRICK), column * (TBY * BRICK), zero_index, zero_index)
        feat_block = lax.dynamic_slice(feat_global, starts, extent)
        grad_block = lax.dynamic_slice(grad_global, starts, extent)
        spots = places[index]
        keep_rows = keeper[index].reshape(-1, 1).astype(jnp.float32)
        grad_rows = grad_masked[index].reshape(-1, C)
        feat_windows = cut_windows(feat_block, spots)
        grad_windows = cut_windows(grad_block, spots)
        output_sum = jnp.zeros((NB * VOX, C), jnp.float32)
        input_sum = jnp.zeros((NB * VOX, C), jnp.float32)
        blocks = []
        for offset in range(OFFS):
            feat_rows = offset_rows(feat_windows, offset)
            output_sum = output_sum + jnp.dot(feat_rows, weight[offset], preferred_element_type=jnp.float32)
            input_sum = input_sum + jnp.dot(offset_rows(grad_windows, offset), weight[OFFS - 1 - offset].T, preferred_element_type=jnp.float32)
            blocks.append(jnp.dot(feat_rows.T, grad_rows, preferred_element_type=jnp.float32))
        output_tile = (output_sum * keep_rows).astype(jnp.bfloat16).reshape(NB, VOX, C)
        input_tile = (input_sum * keep_rows).astype(jnp.bfloat16).reshape(NB, VOX, C)
        return total + jnp.stack(blocks), (output_tile, input_tile)

    indices = jnp.arange(tiles, dtype=jnp.int32)
    total, (outputs, input_grads) = lax.scan(tile_step, jnp.zeros((OFFS, C, C), jnp.float32), indices)
    output = outputs.reshape(TILES_X, TILES_Y, NB, VOX, C)
    input_grad = input_grads.reshape(TILES_X, TILES_Y, NB, VOX, C)
    return output, input_grad, total / jnp.float32(TILES_X * TILES_Y)
```

```python
import jax
import jax.numpy as jnp
from jax import lax
from jax.sharding import PartitionSpec as P

BRICK = 8
TBX = 2
TBY = 2
ZL = 4
OFFS = 27


def with_halo(value, sides, width):
    for axis, dim in sides:
        size, length = (lax.axis_size(axis), value.shape[dim])
        up = [(i, (i + 1) % size) for i in range(size - 1)]
        down = [(j, i) for i, j in up]
        last = lax.slice_in_dim(value, length - width, length, axis=dim)
        leading = lax.slice_in_dim(value, 0, width, axis=dim)
        before = lax.ppermute(last, axis, up)
        after = lax.ppermute(leading, axis, down)
        value = jnp.concatenate([before, value, after], axis=dim)
    return value


STEPS = (("gx", 0), ("gy", 0), ("gx", 2), ("gy", 1), ("gx", 1), ("gx", 3), ("gy", 2), ("gy", 3))


def butterfly_sum(value, steps=STEPS):
    lanes = value.shape[-1]
    flat = value.reshape(-1, lanes)
    rows = flat.shape[0]
    parts = 1 << len(steps)
    padded_rows = -(-rows // parts) * parts
    buf = jnp.pad(flat, ((0, padded_rows - rows), (0, 0)))
    for axis, b in steps:
        half = buf.shape[0] // 2
        pairs = [(i, i ^ (1 << b)) for i in range(lax.axis_size(axis))]
        bit = (lax.axis_index(axis) >> b) & 1
        keep = lax.dynamic_slice_in_dim(buf, bit * half, half, 0)
        send = lax.dynamic_slice_in_dim(buf, (1 - bit) * half, half, 0)
        buf = keep + lax.ppermute(send, axis, pairs)
    for axis, b in reversed(steps):
        pairs = [(i, i ^ (1 << b)) for i in range(lax.axis_size(axis))]
        bit = (lax.axis_index(axis) >> b) & 1
        got = lax.ppermute(buf, axis, pairs)
        buf = jnp.concatenate([jnp.where(bit == 0, buf, got), jnp.where(bit == 0, got, buf)], 0)
    return buf[:rows].reshape(value.shape)


def place_bricks(bricks, places, alive):
    spots = jnp.arange(TBX * TBY * ZL, dtype=jnp.int32)
    picker = ((places[None, :] == spots[:, None]) & alive[None, :]).astype(jnp.bfloat16)
    dense = jnp.einsum("ps,svc->pvc", picker, bricks, preferred_element_type=jnp.float32).astype(
        jnp.bfloat16
    )
    chans = bricks.shape[-1]
    dense = dense.reshape(TBX, TBY, ZL, BRICK, BRICK, BRICK, chans)
    dense = dense.transpose(0, 3, 1, 4, 2, 5, 6)
    return dense.reshape(TBX * BRICK, TBY * BRICK, ZL * BRICK, chans)


def cut_windows(padded, places):
    padded = jnp.pad(padded, ((0, 0), (0, 0), (1, 1), (0, 0)))
    chans = padded.shape[-1]
    along_x = places // (TBY * ZL)
    along_y = places // ZL % TBY
    along_z = places % ZL
    zero_index = jnp.zeros_like(along_x)

    def one_window(start_x, start_y, start_z, start_c):
        return lax.dynamic_slice(
            padded, (start_x, start_y, start_z, start_c), (BRICK + 2, BRICK + 2, BRICK + 2, chans)
        )

    return jax.vmap(one_window)(along_x * BRICK, along_y * BRICK, along_z * BRICK, zero_index)


def offset_rows(windows, offset):
    first = offset // 9
    second = offset // 3 % 3
    third = offset % 3
    piece = windows[:, first : first + BRICK, second : second + BRICK, third : third + BRICK, :]
    return piece.reshape(-1, windows.shape[-1])


def forward_pass(feat_padded, places, weight, keeper_rows):
    feat_windows = cut_windows(feat_padded, places)
    output_sum = jnp.zeros((keeper_rows.shape[0], weight.shape[-1]), jnp.float32)
    for offset in range(OFFS):
        output_sum = output_sum + jnp.dot(
            offset_rows(feat_windows, offset), weight[offset], preferred_element_type=jnp.float32
        )
    return ((output_sum * keeper_rows).astype(jnp.bfloat16), feat_windows)


def local(features, occupancy, brick_pos, brick_count, weight, cotangent):
    slots = features.shape[2]
    chans = features.shape[-1]
    places = brick_pos[0, 0]
    alive = jnp.arange(slots, dtype=jnp.int32) < brick_count[0, 0]
    keeper = (occupancy[0, 0] * alive[:, None].astype(jnp.int32)).astype(jnp.bfloat16)
    keeper_rows = keeper.reshape(-1, 1).astype(jnp.float32)
    feat_masked = features[0, 0] * keeper[:, :, None]
    grad_masked = cotangent[0, 0] * keeper[:, :, None]
    feat_dense = place_bricks(feat_masked, places, alive)
    grad_dense = place_bricks(grad_masked, places, alive)
    feat_padded = with_halo(feat_dense, (("gx", 0), ("gy", 1)), 1)
    output_rows, feat_windows = forward_pass(feat_padded, places, weight, keeper_rows)
    grad_padded = with_halo(grad_dense, (("gx", 0), ("gy", 1)), 1)
    grad_windows = cut_windows(grad_padded, places)
    grad_rows = grad_masked.reshape(-1, chans)
    input_sum = jnp.zeros((grad_rows.shape[0], chans), jnp.float32)
    blocks = []
    for offset in range(OFFS):
        input_sum = input_sum + lax.dot_general(
            offset_rows(grad_windows, offset),
            weight[OFFS - 1 - offset],
            (((1,), (1,)), ((), ())),
            preferred_element_type=jnp.float32,
        )
        blocks.append(
            lax.dot_general(
                offset_rows(feat_windows, offset),
                grad_rows,
                (((0,), (0,)), ((), ())),
                preferred_element_type=jnp.float32,
            )
        )
    weight_local = jnp.stack(blocks)
    input_rows = (input_sum * keeper_rows).astype(jnp.bfloat16)
    tiles = lax.axis_size("gx") * lax.axis_size("gy")
    weight_total = butterfly_sum(weight_local)
    weight_grad = weight_total / jnp.float32(tiles)
    output = output_rows.reshape(1, 1, slots, -1, chans)
    input_grad = input_rows.reshape(1, 1, slots, -1, chans)
    return (output, input_grad, weight_grad)


def solution(mesh):
    return jax.shard_map(
        local,
        mesh=mesh,
        in_specs=(
            P("gx", "gy", None, None, None),
            P("gx", "gy", None, None),
            P("gx", "gy", None),
            P("gx", "gy"),
            P(),
            P("gx", "gy", None, None, None),
        ),
        out_specs=(P("gx", "gy", None, None, None), P("gx", "gy", None, None, None), P()),
        check_vma=False,
    )
```

```python
import jax
import jax.numpy as jnp
from jax import lax
from jax.sharding import PartitionSpec as P

BRICK = 8
TBX = 2
TBY = 2
ZL = 4
OFFS = 27


def with_halo(value, sides, width):
    for axis, dim in sides:
        size, length = (lax.axis_size(axis), value.shape[dim])
        up = [(i, (i + 1) % size) for i in range(size - 1)]
        down = [(j, i) for i, j in up]
        last = lax.slice_in_dim(value, length - width, length, axis=dim)
        leading = lax.slice_in_dim(value, 0, width, axis=dim)
        before = lax.ppermute(last, axis, up)
        after = lax.ppermute(leading, axis, down)
        value = jnp.concatenate([before, value, after], axis=dim)
    return value


STEPS = (("gx", 0), ("gy", 0), ("gx", 2), ("gy", 1), ("gx", 1), ("gx", 3), ("gy", 2), ("gy", 3))


def butterfly_sum(value, steps=STEPS):
    lanes = value.shape[-1]
    flat = value.reshape(-1, lanes)
    rows = flat.shape[0]
    parts = 1 << len(steps)
    padded_rows = -(-rows // parts) * parts
    buf = jnp.pad(flat, ((0, padded_rows - rows), (0, 0)))
    for axis, b in steps:
        half = buf.shape[0] // 2
        pairs = [(i, i ^ (1 << b)) for i in range(lax.axis_size(axis))]
        bit = (lax.axis_index(axis) >> b) & 1
        keep = lax.dynamic_slice_in_dim(buf, bit * half, half, 0)
        send = lax.dynamic_slice_in_dim(buf, (1 - bit) * half, half, 0)
        buf = keep + lax.ppermute(send, axis, pairs)
    for axis, b in reversed(steps):
        pairs = [(i, i ^ (1 << b)) for i in range(lax.axis_size(axis))]
        bit = (lax.axis_index(axis) >> b) & 1
        got = lax.ppermute(buf, axis, pairs)
        buf = jnp.concatenate([jnp.where(bit == 0, buf, got), jnp.where(bit == 0, got, buf)], 0)
    return buf[:rows].reshape(value.shape)


def place_bricks(bricks, places, alive):
    spots = jnp.arange(TBX * TBY * ZL, dtype=jnp.int32)
    picker = ((places[None, :] == spots[:, None]) & alive[None, :]).astype(jnp.bfloat16)
    dense = jnp.einsum("ps,svc->pvc", picker, bricks, preferred_element_type=jnp.float32).astype(
        jnp.bfloat16
    )
    chans = bricks.shape[-1]
    dense = dense.reshape(TBX, TBY, ZL, BRICK, BRICK, BRICK, chans)
    dense = dense.transpose(0, 3, 1, 4, 2, 5, 6)
    return dense.reshape(TBX * BRICK, TBY * BRICK, ZL * BRICK, chans)


def cut_windows(padded, places):
    padded = jnp.pad(padded, ((0, 0), (0, 0), (1, 1), (0, 0)))
    chans = padded.shape[-1]
    windows = []
    for slot in range(places.shape[0]):
        place = places[slot]
        starts = (place // (TBY * ZL) * BRICK, place // ZL % TBY * BRICK, place % ZL * BRICK, 0)
        windows.append(lax.dynamic_slice(padded, starts, (BRICK + 2, BRICK + 2, BRICK + 2, chans)))
    return jnp.stack(windows)


def stack_offsets(windows):
    pieces = []
    for offset in range(OFFS):
        first, second, third = offset // 9, offset // 3 % 3, offset % 3
        piece = windows[:, first : first + BRICK, second : second + BRICK, third : third + BRICK, :]
        pieces.append(piece.reshape(-1, windows.shape[-1]))
    return jnp.stack(pieces)


def local(features, occupancy, brick_pos, brick_count, weight, cotangent):
    slots = features.shape[2]
    chans = features.shape[-1]
    places = brick_pos[0, 0]
    alive = jnp.arange(slots, dtype=jnp.int32) < brick_count[0, 0]
    keeper = (occupancy[0, 0] * alive[:, None].astype(jnp.int32)).astype(jnp.bfloat16)
    keeper_rows = keeper.reshape(-1, 1).astype(jnp.float32)
    feat_masked = features[0, 0] * keeper[:, :, None]
    grad_masked = cotangent[0, 0] * keeper[:, :, None]
    grad_rows = grad_masked.reshape(-1, chans)
    feat_dense = place_bricks(feat_masked, places, alive)
    feat_padded = with_halo(feat_dense, (("gx", 0), ("gy", 1)), 1)
    feat_stack = stack_offsets(cut_windows(feat_padded, places))
    weight_local = jnp.einsum("dvc,ve->dce", feat_stack, grad_rows, preferred_element_type=jnp.float32)
    tiles = lax.axis_size("gx") * lax.axis_size("gy")
    weight_total = butterfly_sum(weight_local)
    weight_grad = weight_total / jnp.float32(tiles)
    output_sum = jnp.einsum("dvc,dce->ve", feat_stack, weight, preferred_element_type=jnp.float32)
    output_rows = (output_sum * keeper_rows).astype(jnp.bfloat16)
    grad_dense = place_bricks(grad_masked, places, alive)
    grad_padded = with_halo(grad_dense, (("gx", 0), ("gy", 1)), 1)
    grad_stack = stack_offsets(cut_windows(grad_padded, places))
    input_sum = jnp.einsum("dvc,dec->ve", grad_stack, weight[::-1], preferred_element_type=jnp.float32)
    input_rows = (input_sum * keeper_rows).astype(jnp.bfloat16)
    output = output_rows.reshape(1, 1, slots, -1, chans)
    input_grad = input_rows.reshape(1, 1, slots, -1, chans)
    return (output, input_grad, weight_grad)


def solution(mesh):
    return jax.shard_map(
        local,
        mesh=mesh,
        in_specs=(
            P("gx", "gy", None, None, None),
            P("gx", "gy", None, None),
            P("gx", "gy", None),
            P("gx", "gy"),
            P(),
            P("gx", "gy", None, None, None),
        ),
        out_specs=(P("gx", "gy", None, None, None), P("gx", "gy", None, None, None), P()),
        check_vma=False,
    )
```

```python
import jax
import jax.numpy as jnp
from jax import lax
from jax.sharding import PartitionSpec as P

BRICK = 8
TBX = 2
TBY = 2
ZL = 4
OFFS = 27


def with_halo(value, sides, width):
    for axis, dim in sides:
        size, length = (lax.axis_size(axis), value.shape[dim])
        up = [(i, (i + 1) % size) for i in range(size - 1)]
        down = [(j, i) for i, j in up]
        last = lax.slice_in_dim(value, length - width, length, axis=dim)
        leading = lax.slice_in_dim(value, 0, width, axis=dim)
        before = lax.ppermute(last, axis, up)
        after = lax.ppermute(leading, axis, down)
        value = jnp.concatenate([before, value, after], axis=dim)
    return value


STEPS = (("gx", 0), ("gy", 0), ("gx", 2), ("gy", 1), ("gx", 1), ("gx", 3), ("gy", 2), ("gy", 3))


def butterfly_scatter(value, steps=STEPS):
    lanes = value.shape[-1]
    flat = value.reshape(-1, lanes)
    rows = flat.shape[0]
    parts = 1 << len(steps)
    padded_rows = -(-rows // parts) * parts
    buf = jnp.pad(flat, ((0, padded_rows - rows), (0, 0)))
    for axis, b in steps:
        half = buf.shape[0] // 2
        pairs = [(i, i ^ (1 << b)) for i in range(lax.axis_size(axis))]
        bit = (lax.axis_index(axis) >> b) & 1
        keep = lax.dynamic_slice_in_dim(buf, bit * half, half, 0)
        send = lax.dynamic_slice_in_dim(buf, (1 - bit) * half, half, 0)
        buf = keep + lax.ppermute(send, axis, pairs)
    return buf


def butterfly_gather(buf, like, steps=STEPS):
    for axis, b in reversed(steps):
        pairs = [(i, i ^ (1 << b)) for i in range(lax.axis_size(axis))]
        bit = (lax.axis_index(axis) >> b) & 1
        got = lax.ppermute(buf, axis, pairs)
        buf = jnp.concatenate([jnp.where(bit == 0, buf, got), jnp.where(bit == 0, got, buf)], 0)
    return buf[: like.size // like.shape[-1]].reshape(like.shape)


def place_bricks(bricks, places, alive):
    spots = jnp.arange(TBX * TBY * ZL, dtype=jnp.int32)
    picker = ((places[None, :] == spots[:, None]) & alive[None, :]).astype(jnp.bfloat16)
    dense = jnp.einsum("ps,tsvc->tpvc", picker, bricks, preferred_element_type=jnp.float32).astype(
        jnp.bfloat16
    )
    kinds, chans = bricks.shape[0], bricks.shape[-1]
    dense = dense.reshape(kinds, TBX, TBY, ZL, BRICK, BRICK, BRICK, chans)
    dense = dense.transpose(0, 1, 4, 2, 5, 3, 6, 7)
    return dense.reshape(kinds, TBX * BRICK, TBY * BRICK, ZL * BRICK, chans)


def cut_windows(padded, places):
    padded = jnp.pad(padded, ((0, 0), (0, 0), (0, 0), (1, 1), (0, 0)))
    kinds, chans = padded.shape[0], padded.shape[-1]
    windows = []
    for slot in range(places.shape[0]):
        place = places[slot]
        starts = (0, place // (TBY * ZL) * BRICK, place // ZL % TBY * BRICK, place % ZL * BRICK, 0)
        windows.append(
            lax.dynamic_slice(padded, starts, (kinds, BRICK + 2, BRICK + 2, BRICK + 2, chans))
        )
    return jnp.stack(windows, 1)


def stack_offsets(windows):
    pieces = []
    for offset in range(OFFS):
        first, second, third = offset // 9, offset // 3 % 3, offset % 3
        piece = windows[:, first : first + BRICK, second : second + BRICK, third : third + BRICK, :]
        pieces.append(piece.reshape(-1, windows.shape[-1]))
    return jnp.stack(pieces)


def local(features, occupancy, brick_pos, brick_count, weight, cotangent):
    slots = features.shape[2]
    chans = features.shape[-1]
    places = brick_pos[0, 0]
    alive = jnp.arange(slots, dtype=jnp.int32) < brick_count[0, 0]
    keeper = (occupancy[0, 0] * alive[:, None].astype(jnp.int32)).astype(jnp.bfloat16)
    keeper_rows = keeper.reshape(-1, 1).astype(jnp.float32)
    both = jnp.stack([features[0, 0], cotangent[0, 0]]) * keeper[None, :, :, None]
    grad_rows = both[1].reshape(-1, chans)
    dense = place_bricks(both, places, alive)
    padded = with_halo(dense, (("gx", 1), ("gy", 2)), 1)
    windows = cut_windows(padded, places)
    feat_stack = stack_offsets(windows[0])
    weight_local = jnp.einsum("ve,dvc->edc", grad_rows, feat_stack, preferred_element_type=jnp.float32)
    tiles = lax.axis_size("gx") * lax.axis_size("gy")
    half_done = butterfly_scatter(weight_local)
    output_sum = jnp.einsum("dvc,dce->ve", feat_stack, weight, preferred_element_type=jnp.float32)
    output_rows = (output_sum * keeper_rows).astype(jnp.bfloat16)
    grad_stack = stack_offsets(windows[1])
    input_sum = jnp.einsum("dvc,dec->ve", grad_stack, weight[::-1], preferred_element_type=jnp.float32)
    input_rows = (input_sum * keeper_rows).astype(jnp.bfloat16)
    half_done, output_rows, input_rows = lax.optimization_barrier((half_done, output_rows, input_rows))
    weight_total = butterfly_gather(half_done, weight_local)
    weight_grad = weight_total.transpose(1, 2, 0) / jnp.float32(tiles)
    output = output_rows.reshape(1, 1, slots, -1, chans)
    input_grad = input_rows.reshape(1, 1, slots, -1, chans)
    return (output, input_grad, weight_grad)


def solution(mesh):
    return jax.shard_map(
        local,
        mesh=mesh,
        in_specs=(
            P("gx", "gy", None, None, None),
            P("gx", "gy", None, None),
            P("gx", "gy", None),
            P("gx", "gy"),
            P(),
            P("gx", "gy", None, None, None),
        ),
        out_specs=(P("gx", "gy", None, None, None), P("gx", "gy", None, None, None), P()),
        check_vma=False,
    )
```

```python
import jax
import jax.numpy as jnp
from jax import lax
from jax.sharding import PartitionSpec as P

BRICK = 8
TBX = 2
TBY = 2
ZL = 4
OFFS = 27


def with_halo(value, sides):
    pads = [(0, 0)] * value.ndim
    for _, dim in sides:
        pads[dim] = (1, 1)
    pads[-2] = (1, 1)
    padded = jnp.pad(value, pads)
    for axis, dim in sides:
        size, length = lax.axis_size(axis), padded.shape[dim]
        up = [(i, (i + 1) % size) for i in range(size - 1)]
        down = [(j, i) for i, j in up]
        last = lax.slice_in_dim(padded, length - 2, length - 1, axis=dim)
        leading = lax.slice_in_dim(padded, 1, 2, axis=dim)
        padded = lax.dynamic_update_slice_in_dim(padded, lax.ppermute(last, axis, up), 0, axis=dim)
        padded = lax.dynamic_update_slice_in_dim(
            padded, lax.ppermute(leading, axis, down), length - 1, axis=dim
        )
    return padded


STEPS = (("gx", 0), ("gy", 0), ("gx", 2), ("gy", 1), ("gx", 1), ("gx", 3), ("gy", 2), ("gy", 3))


def butterfly_scatter(value, steps=STEPS):
    lanes = value.shape[-1]
    flat = value.reshape(-1, lanes)
    rows = flat.shape[0]
    parts = 1 << len(steps)
    padded_rows = -(-rows // parts) * parts
    buf = jnp.pad(flat, ((0, padded_rows - rows), (0, 0)))
    for axis, b in steps:
        half = buf.shape[0] // 2
        pairs = [(i, i ^ (1 << b)) for i in range(lax.axis_size(axis))]
        bit = (lax.axis_index(axis) >> b) & 1
        keep = lax.dynamic_slice_in_dim(buf, bit * half, half, 0)
        send = lax.dynamic_slice_in_dim(buf, (1 - bit) * half, half, 0)
        buf = keep + lax.ppermute(send, axis, pairs)
    return buf


def butterfly_gather(buf, like, steps=STEPS):
    for axis, b in reversed(steps):
        pairs = [(i, i ^ (1 << b)) for i in range(lax.axis_size(axis))]
        bit = (lax.axis_index(axis) >> b) & 1
        got = lax.ppermute(buf, axis, pairs)
        buf = jnp.concatenate([jnp.where(bit == 0, buf, got), jnp.where(bit == 0, got, buf)], 0)
    return buf[: like.size // like.shape[-1]].reshape(like.shape)


def place_bricks(bricks, places, alive):
    spots = jnp.arange(TBX * TBY * ZL, dtype=jnp.int32)
    picker = ((places[None, :] == spots[:, None]) & alive[None, :]).astype(jnp.bfloat16)
    dense = jnp.einsum("ps,tsvc->tpvc", picker, bricks, preferred_element_type=jnp.float32).astype(
        jnp.bfloat16
    )
    kinds, chans = bricks.shape[0], bricks.shape[-1]
    dense = dense.reshape(kinds, TBX, TBY, ZL, BRICK, BRICK, BRICK, chans)
    dense = dense.transpose(0, 1, 4, 2, 5, 3, 6, 7)
    return dense.reshape(kinds, TBX * BRICK, TBY * BRICK, ZL * BRICK, chans)


def cut_windows(padded, places):
    kinds, chans = padded.shape[0], padded.shape[-1]
    windows = []
    for slot in range(places.shape[0]):
        place = places[slot]
        starts = (0, place // (TBY * ZL) * BRICK, place // ZL % TBY * BRICK, place % ZL * BRICK, 0)
        windows.append(
            lax.dynamic_slice(padded, starts, (kinds, BRICK + 2, BRICK + 2, BRICK + 2, chans))
        )
    return jnp.stack(windows, 1)


def stack_offsets(windows):
    pieces = []
    for offset in range(OFFS):
        first, second, third = offset // 9, offset // 3 % 3, offset % 3
        piece = windows[:, first : first + BRICK, second : second + BRICK, third : third + BRICK, :]
        pieces.append(piece.reshape(-1, windows.shape[-1]))
    return jnp.stack(pieces)


def local(features, occupancy, brick_pos, brick_count, weight, cotangent):
    slots = features.shape[2]
    chans = features.shape[-1]
    places = brick_pos[0, 0]
    alive = jnp.arange(slots, dtype=jnp.int32) < brick_count[0, 0]
    keeper = (occupancy[0, 0] * alive[:, None].astype(jnp.int32)).astype(jnp.bfloat16)
    keeper_rows = keeper.reshape(-1, 1).astype(jnp.float32)
    both = jnp.stack([features[0, 0], cotangent[0, 0]]) * keeper[None, :, :, None]
    grad_rows = both[1].reshape(-1, chans)
    dense = place_bricks(both, places, alive)
    padded = with_halo(dense, (("gx", 1), ("gy", 2)))
    windows = cut_windows(padded, places)
    feat_stack = stack_offsets(windows[0])
    tiles = lax.axis_size("gx") * lax.axis_size("gy")
    weight_local = jnp.einsum("ve,dvc->dec", grad_rows, feat_stack, preferred_element_type=jnp.float32)
    weight_local = weight_local * jnp.float32(1.0 / tiles)
    half_done = butterfly_scatter(weight_local)
    output_sum = jnp.einsum("dvc,dce->ve", feat_stack, weight, preferred_element_type=jnp.float32)
    output_rows = (output_sum * keeper_rows).astype(jnp.bfloat16)
    grad_stack = stack_offsets(windows[1])
    input_sum = jnp.einsum("dvc,dec->ve", grad_stack, weight[::-1], preferred_element_type=jnp.float32)
    input_rows = (input_sum * keeper_rows).astype(jnp.bfloat16)
    half_done, output_rows, input_rows = lax.optimization_barrier((half_done, output_rows, input_rows))
    weight_total = butterfly_gather(half_done, weight_local)
    weight_grad = weight_total.transpose(0, 2, 1)
    output = output_rows.reshape(1, 1, slots, -1, chans)
    input_grad = input_rows.reshape(1, 1, slots, -1, chans)
    return (output, input_grad, weight_grad)


def solution(mesh):
    return jax.shard_map(
        local,
        mesh=mesh,
        in_specs=(
            P("gx", "gy", None, None, None),
            P("gx", "gy", None, None),
            P("gx", "gy", None),
            P("gx", "gy"),
            P(),
            P("gx", "gy", None, None, None),
        ),
        out_specs=(P("gx", "gy", None, None, None), P("gx", "gy", None, None, None), P()),
        check_vma=False,
    )
```

```python
import jax
import jax.numpy as jnp
from jax import lax
from jax.sharding import PartitionSpec as P

BRICK = 8
TBX = 2
TBY = 2
ZL = 4
OFFS = 27


ZPAD = 8


def shift_pairs(size_x, size_y, dx, dy):
    pairs = []
    for i in range(size_x):
        for j in range(size_y):
            if 0 <= i + dx < size_x and 0 <= j + dy < size_y:
                pairs.append((i * size_y + j, (i + dx) * size_y + j + dy))
    return pairs


def with_halo(value):
    kinds, nx, ny, nz, chans = value.shape
    padded = jnp.pad(value, ((0, 0), (1, 1), (1, 1), (ZPAD, ZPAD), (0, 0)))
    sx, sy = lax.axis_size("gx"), lax.axis_size("gy")
    zs = slice(ZPAD, ZPAD + nz)
    pieces = []
    for dx, dy in ((1, 0), (-1, 0), (0, 1), (0, -1), (1, 1), (1, -1), (-1, 1), (-1, -1)):
        xs = slice(nx, nx + 1) if dx > 0 else (slice(1, 2) if dx < 0 else slice(0, nx + 2))
        ys = slice(ny, ny + 1) if dy > 0 else (slice(1, 2) if dy < 0 else slice(0, ny + 2))
        face = padded[:, xs, ys, zs, :]
        got = lax.ppermute(face, ("gx", "gy"), shift_pairs(sx, sy, dx, dy))
        at_x = 0 if dx > 0 else (nx + 1 if dx < 0 else 0)
        at_y = 0 if dy > 0 else (ny + 1 if dy < 0 else 0)
        pieces.append((got, at_x, at_y))
    for got, at_x, at_y in pieces:
        padded = lax.dynamic_update_slice(padded, got, (0, at_x, at_y, ZPAD, 0))
    return padded


STEPS = (("gx", 0), ("gy", 0), ("gx", 2), ("gy", 1), ("gx", 1), ("gx", 3), ("gy", 2), ("gy", 3))


def butterfly_scatter(value, steps=STEPS):
    lanes = value.shape[-1]
    flat = value.reshape(-1, lanes)
    rows = flat.shape[0]
    parts = 1 << len(steps)
    padded_rows = -(-rows // parts) * parts
    buf = jnp.pad(flat, ((0, padded_rows - rows), (0, 0)))
    for axis, b in steps:
        half = buf.shape[0] // 2
        pairs = [(i, i ^ (1 << b)) for i in range(lax.axis_size(axis))]
        bit = (lax.axis_index(axis) >> b) & 1
        keep = lax.dynamic_slice_in_dim(buf, bit * half, half, 0)
        send = lax.dynamic_slice_in_dim(buf, (1 - bit) * half, half, 0)
        buf = keep + lax.ppermute(send, axis, pairs)
    return buf


def butterfly_gather(buf, like, steps=STEPS):
    for axis, b in reversed(steps):
        pairs = [(i, i ^ (1 << b)) for i in range(lax.axis_size(axis))]
        bit = (lax.axis_index(axis) >> b) & 1
        got = lax.ppermute(buf, axis, pairs)
        buf = jnp.concatenate([jnp.where(bit == 0, buf, got), jnp.where(bit == 0, got, buf)], 0)
    return buf[: like.size // like.shape[-1]].reshape(like.shape)


def place_bricks(bricks, places, alive):
    spots = jnp.arange(TBX * TBY * ZL, dtype=jnp.int32)
    picker = ((places[None, :] == spots[:, None]) & alive[None, :]).astype(jnp.bfloat16)
    dense = jnp.einsum("ps,tsvc->tpvc", picker, bricks, preferred_element_type=jnp.float32).astype(
        jnp.bfloat16
    )
    kinds, chans = bricks.shape[0], bricks.shape[-1]
    dense = dense.reshape(kinds, TBX, TBY, ZL, BRICK, BRICK, BRICK, chans)
    dense = dense.transpose(0, 1, 4, 2, 5, 3, 6, 7)
    return dense.reshape(kinds, TBX * BRICK, TBY * BRICK, ZL * BRICK, chans)


def cut_windows(padded, places):
    kinds, chans = padded.shape[0], padded.shape[-1]
    windows = []
    for slot in range(places.shape[0]):
        place = places[slot]
        starts = (0, place // (TBY * ZL) * BRICK, place // ZL % TBY * BRICK, place % ZL * BRICK + ZPAD - 1, 0)
        windows.append(
            lax.dynamic_slice(padded, starts, (kinds, BRICK + 2, BRICK + 2, BRICK + 2, chans))
        )
    return jnp.stack(windows, 1)


def stack_offsets(windows):
    pieces = []
    for offset in range(OFFS):
        first, second, third = offset // 9, offset // 3 % 3, offset % 3
        piece = windows[:, first : first + BRICK, second : second + BRICK, third : third + BRICK, :]
        pieces.append(piece.reshape(-1, windows.shape[-1]))
    return jnp.stack(pieces)


def local(features, occupancy, brick_pos, brick_count, weight, cotangent):
    slots = features.shape[2]
    chans = features.shape[-1]
    places = brick_pos[0, 0]
    alive = jnp.arange(slots, dtype=jnp.int32) < brick_count[0, 0]
    keeper = (occupancy[0, 0] * alive[:, None].astype(jnp.int32)).astype(jnp.bfloat16)
    keeper_rows = keeper.reshape(-1, 1).astype(jnp.float32)
    both = jnp.stack([features[0, 0], cotangent[0, 0]]) * keeper[None, :, :, None]
    grad_rows = both[1].reshape(-1, chans)
    dense = place_bricks(both, places, alive)
    padded = with_halo(dense)
    windows = cut_windows(padded, places)
    feat_stack = stack_offsets(windows[0])
    tiles = lax.axis_size("gx") * lax.axis_size("gy")
    weight_local = jnp.einsum("ve,dvc->dec", grad_rows, feat_stack, preferred_element_type=jnp.float32)
    weight_local = weight_local * jnp.float32(1.0 / tiles)
    half_done = butterfly_scatter(weight_local)
    output_sum = jnp.einsum("dvc,dce->ve", feat_stack, weight, preferred_element_type=jnp.float32)
    output_rows = (output_sum * keeper_rows).astype(jnp.bfloat16)
    grad_stack = stack_offsets(windows[1])
    input_sum = jnp.einsum("dvc,dec->ve", grad_stack, weight[::-1], preferred_element_type=jnp.float32)
    input_rows = (input_sum * keeper_rows).astype(jnp.bfloat16)
    half_done, output_rows, input_rows = lax.optimization_barrier((half_done, output_rows, input_rows))
    weight_total = butterfly_gather(half_done, weight_local)
    weight_grad = weight_total.transpose(0, 2, 1)
    output = output_rows.reshape(1, 1, slots, -1, chans)
    input_grad = input_rows.reshape(1, 1, slots, -1, chans)
    return (output, input_grad, weight_grad)


def solution(mesh):
    return jax.shard_map(
        local,
        mesh=mesh,
        in_specs=(
            P("gx", "gy", None, None, None),
            P("gx", "gy", None, None),
            P("gx", "gy", None),
            P("gx", "gy"),
            P(),
            P("gx", "gy", None, None, None),
        ),
        out_specs=(P("gx", "gy", None, None, None), P("gx", "gy", None, None, None), P()),
        check_vma=False,
    )
```

```python
import jax
import jax.numpy as jnp
from jax import lax
from jax.sharding import PartitionSpec as P

BRICK = 8
TBX = 2
TBY = 2
ZL = 4
OFFS = 27


def with_halo(value, sides):
    pads = [(0, 0)] * value.ndim
    for _, dim in sides:
        pads[dim] = (1, 1)
    pads[-2] = (1, 1)
    padded = jnp.pad(value, pads)
    for axis, dim in sides:
        size, length = lax.axis_size(axis), padded.shape[dim]
        up = [(i, (i + 1) % size) for i in range(size - 1)]
        down = [(j, i) for i, j in up]
        last = lax.slice_in_dim(padded, length - 2, length - 1, axis=dim)
        leading = lax.slice_in_dim(padded, 1, 2, axis=dim)
        padded = lax.dynamic_update_slice_in_dim(padded, lax.ppermute(last, axis, up), 0, axis=dim)
        padded = lax.dynamic_update_slice_in_dim(
            padded, lax.ppermute(leading, axis, down), length - 1, axis=dim
        )
    return padded


FIRST = ("gx", 0)
ORDERS = (
    (("gy", 0), ("gx", 2), ("gy", 1), ("gx", 1), ("gx", 3), ("gy", 2), ("gy", 3)),
    (("gx", 2), ("gy", 1), ("gy", 0), ("gx", 3), ("gy", 2), ("gx", 1), ("gy", 3)),
)


def step_bit(step):
    axis, b = step
    return (lax.axis_index(axis) >> b) & 1


def step_pairs(k):
    sx, sy = lax.axis_size("gx"), lax.axis_size("gy")
    pairs = []
    for i in range(sx):
        for j in range(sy):
            axis, b = ORDERS[i & 1][k]
            pi, pj = (i ^ (1 << b), j) if axis == "gx" else (i, j ^ (1 << b))
            pairs.append((i * sy + j, pi * sy + pj))
    return pairs


def core_bit(k):
    return jnp.where(lax.axis_index("gx") & 1 == 0, step_bit(ORDERS[0][k]), step_bit(ORDERS[1][k]))


def butterfly_scatter(value):
    lanes = value.shape[-1]
    flat = value.reshape(-1, lanes)
    rows = flat.shape[0]
    parts = 1 << (1 + len(ORDERS[0]))
    padded_rows = -(-rows // parts) * parts
    buf = jnp.pad(flat, ((0, padded_rows - rows), (0, 0)))
    half = buf.shape[0] // 2
    bit = step_bit(FIRST)
    pairs = [(i, i ^ 1) for i in range(lax.axis_size("gx"))]
    keep = lax.dynamic_slice_in_dim(buf, bit * half, half, 0)
    send = lax.dynamic_slice_in_dim(buf, (1 - bit) * half, half, 0)
    buf = keep + lax.ppermute(send, "gx", pairs)
    for k in range(len(ORDERS[0])):
        half = buf.shape[0] // 2
        bit = core_bit(k)
        keep = lax.dynamic_slice_in_dim(buf, bit * half, half, 0)
        send = lax.dynamic_slice_in_dim(buf, (1 - bit) * half, half, 0)
        buf = keep + lax.ppermute(send, ("gx", "gy"), step_pairs(k))
    return buf


def join_halves(buf, got, bit):
    return jnp.concatenate([jnp.where(bit == 0, buf, got), jnp.where(bit == 0, got, buf)], 0)


def butterfly_gather(buf, like):
    for k in reversed(range(len(ORDERS[0]))):
        got = lax.ppermute(buf, ("gx", "gy"), step_pairs(k))
        buf = join_halves(buf, got, core_bit(k))
    got = lax.ppermute(buf, "gx", [(i, i ^ 1) for i in range(lax.axis_size("gx"))])
    buf = join_halves(buf, got, step_bit(FIRST))
    return buf[: like.size // like.shape[-1]].reshape(like.shape)


def place_bricks(bricks, places, alive):
    spots = jnp.arange(TBX * TBY * ZL, dtype=jnp.int32)
    picker = ((places[None, :] == spots[:, None]) & alive[None, :]).astype(jnp.bfloat16)
    dense = jnp.einsum("ps,tsvc->tpvc", picker, bricks, preferred_element_type=jnp.float32).astype(
        jnp.bfloat16
    )
    kinds, chans = bricks.shape[0], bricks.shape[-1]
    dense = dense.reshape(kinds, TBX, TBY, ZL, BRICK, BRICK, BRICK, chans)
    dense = dense.transpose(0, 1, 4, 2, 5, 3, 6, 7)
    return dense.reshape(kinds, TBX * BRICK, TBY * BRICK, ZL * BRICK, chans)


def cut_windows(padded, places):
    kinds, chans = padded.shape[0], padded.shape[-1]
    windows = []
    for slot in range(places.shape[0]):
        place = places[slot]
        starts = (0, place // (TBY * ZL) * BRICK, place // ZL % TBY * BRICK, place % ZL * BRICK, 0)
        windows.append(
            lax.dynamic_slice(padded, starts, (kinds, BRICK + 2, BRICK + 2, BRICK + 2, chans))
        )
    return jnp.stack(windows, 1)


def stack_offsets(windows):
    pieces = []
    for offset in range(OFFS):
        first, second, third = offset // 9, offset // 3 % 3, offset % 3
        piece = windows[:, first : first + BRICK, second : second + BRICK, third : third + BRICK, :]
        pieces.append(piece.reshape(-1, windows.shape[-1]))
    return jnp.stack(pieces)


def local(features, occupancy, brick_pos, brick_count, weight, cotangent):
    slots = features.shape[2]
    chans = features.shape[-1]
    places = brick_pos[0, 0]
    alive = jnp.arange(slots, dtype=jnp.int32) < brick_count[0, 0]
    keeper = (occupancy[0, 0] * alive[:, None].astype(jnp.int32)).astype(jnp.bfloat16)
    keeper_rows = keeper.reshape(-1, 1).astype(jnp.float32)
    both = jnp.stack([features[0, 0], cotangent[0, 0]]) * keeper[None, :, :, None]
    grad_rows = both[1].reshape(-1, chans)
    dense = place_bricks(both, places, alive)
    padded = with_halo(dense, (("gx", 1), ("gy", 2)))
    windows = cut_windows(padded, places)
    feat_stack = stack_offsets(windows[0])
    tiles = lax.axis_size("gx") * lax.axis_size("gy")
    weight_local = jnp.einsum("ve,dvc->dec", grad_rows, feat_stack, preferred_element_type=jnp.float32)
    weight_local = weight_local * jnp.float32(1.0 / tiles)
    half_done = butterfly_scatter(weight_local)
    output_sum = jnp.einsum("dvc,dce->ve", feat_stack, weight, preferred_element_type=jnp.float32)
    output_rows = (output_sum * keeper_rows).astype(jnp.bfloat16)
    grad_stack = stack_offsets(windows[1])
    input_sum = jnp.einsum("dvc,dec->ve", grad_stack, weight[::-1], preferred_element_type=jnp.float32)
    input_rows = (input_sum * keeper_rows).astype(jnp.bfloat16)
    half_done, output_rows, input_rows = lax.optimization_barrier((half_done, output_rows, input_rows))
    weight_total = butterfly_gather(half_done, weight_local)
    weight_grad = weight_total.transpose(0, 2, 1)
    output = output_rows.reshape(1, 1, slots, -1, chans)
    input_grad = input_rows.reshape(1, 1, slots, -1, chans)
    return (output, input_grad, weight_grad)


def solution(mesh):
    return jax.shard_map(
        local,
        mesh=mesh,
        in_specs=(
            P("gx", "gy", None, None, None),
            P("gx", "gy", None, None),
            P("gx", "gy", None),
            P("gx", "gy"),
            P(),
            P("gx", "gy", None, None, None),
        ),
        out_specs=(P("gx", "gy", None, None, None), P("gx", "gy", None, None, None), P()),
        check_vma=False,
    )
```

```python
import jax
import jax.numpy as jnp
from jax import lax
from jax.sharding import PartitionSpec as P

BRICK = 8
TBX = 2
TBY = 2
ZL = 4
OFFS = 27


def with_halo(value):
    nx, ny = value.shape[1], value.shape[2]
    size_x, size_y = lax.axis_size("gx"), lax.axis_size("gy")
    up_x = [(i, i + 1) for i in range(size_x - 1)]
    up_y = [(i, i + 1) for i in range(size_y - 1)]
    down_x = [(j, i) for i, j in up_x]
    down_y = [(j, i) for i, j in up_y]
    from_left = lax.ppermute(value[:, nx - 1 : nx], "gx", up_x)
    from_right = lax.ppermute(value[:, 0:1], "gx", down_x)
    padded = jnp.pad(value, ((0, 0), (1, 1), (1, 1), (1, 1), (0, 0)))

    def row(at):
        return jnp.concatenate([from_left[:, :, at], value[:, :, at], from_right[:, :, at]], 1)

    from_below = lax.ppermute(row(slice(ny - 1, ny)), "gy", up_y)
    from_above = lax.ppermute(row(slice(0, 1)), "gy", down_y)
    padded = lax.dynamic_update_slice(padded, from_left, (0, 0, 1, 1, 0))
    padded = lax.dynamic_update_slice(padded, from_right, (0, nx + 1, 1, 1, 0))
    padded = lax.dynamic_update_slice(padded, from_below, (0, 0, 0, 1, 0))
    padded = lax.dynamic_update_slice(padded, from_above, (0, 0, ny + 1, 1, 0))
    return padded


FIRST = ("gx", 0)
ORDERS = (
    (("gy", 0), ("gx", 2), ("gy", 1), ("gx", 1), ("gx", 3), ("gy", 2), ("gy", 3)),
    (("gx", 2), ("gy", 1), ("gy", 0), ("gx", 3), ("gy", 2), ("gx", 1), ("gy", 3)),
)


def step_bit(step):
    axis, b = step
    return (lax.axis_index(axis) >> b) & 1


def step_pairs(k):
    sx, sy = lax.axis_size("gx"), lax.axis_size("gy")
    pairs = []
    for i in range(sx):
        for j in range(sy):
            axis, b = ORDERS[i & 1][k]
            pi, pj = (i ^ (1 << b), j) if axis == "gx" else (i, j ^ (1 << b))
            pairs.append((i * sy + j, pi * sy + pj))
    return pairs


def core_bit(k):
    return jnp.where(lax.axis_index("gx") & 1 == 0, step_bit(ORDERS[0][k]), step_bit(ORDERS[1][k]))


def butterfly_scatter(value):
    lanes = value.shape[-1]
    flat = value.reshape(-1, lanes)
    rows = flat.shape[0]
    parts = 1 << (1 + len(ORDERS[0]))
    padded_rows = -(-rows // parts) * parts
    buf = jnp.pad(flat, ((0, padded_rows - rows), (0, 0)))
    half = buf.shape[0] // 2
    bit = step_bit(FIRST)
    pairs = [(i, i ^ 1) for i in range(lax.axis_size("gx"))]
    keep = lax.dynamic_slice_in_dim(buf, bit * half, half, 0)
    send = lax.dynamic_slice_in_dim(buf, (1 - bit) * half, half, 0)
    buf = keep + lax.ppermute(send, "gx", pairs)
    for k in range(len(ORDERS[0])):
        half = buf.shape[0] // 2
        bit = core_bit(k)
        keep = lax.dynamic_slice_in_dim(buf, bit * half, half, 0)
        send = lax.dynamic_slice_in_dim(buf, (1 - bit) * half, half, 0)
        buf = keep + lax.ppermute(send, ("gx", "gy"), step_pairs(k))
    return buf


def join_halves(buf, got, bit):
    return jnp.concatenate([jnp.where(bit == 0, buf, got), jnp.where(bit == 0, got, buf)], 0)


def butterfly_gather(buf, like):
    for k in reversed(range(len(ORDERS[0]))):
        got = lax.ppermute(buf, ("gx", "gy"), step_pairs(k))
        buf = join_halves(buf, got, core_bit(k))
    got = lax.ppermute(buf, "gx", [(i, i ^ 1) for i in range(lax.axis_size("gx"))])
    buf = join_halves(buf, got, step_bit(FIRST))
    return buf[: like.size // like.shape[-1]].reshape(like.shape)


def place_bricks(bricks, places, alive):
    spots = jnp.arange(TBX * TBY * ZL, dtype=jnp.int32)
    picker = ((places[None, :] == spots[:, None]) & alive[None, :]).astype(jnp.bfloat16)
    dense = jnp.einsum("ps,tsvc->tpvc", picker, bricks, preferred_element_type=jnp.float32).astype(
        jnp.bfloat16
    )
    kinds, chans = bricks.shape[0], bricks.shape[-1]
    dense = dense.reshape(kinds, TBX, TBY, ZL, BRICK, BRICK, BRICK, chans)
    dense = dense.transpose(0, 1, 4, 2, 5, 3, 6, 7)
    return dense.reshape(kinds, TBX * BRICK, TBY * BRICK, ZL * BRICK, chans)


def cut_windows(padded, places):
    kinds, chans = padded.shape[0], padded.shape[-1]
    windows = []
    for slot in range(places.shape[0]):
        place = places[slot]
        starts = (0, place // (TBY * ZL) * BRICK, place // ZL % TBY * BRICK, place % ZL * BRICK, 0)
        windows.append(
            lax.dynamic_slice(padded, starts, (kinds, BRICK + 2, BRICK + 2, BRICK + 2, chans))
        )
    return jnp.stack(windows, 1)


def stack_offsets(windows):
    pieces = []
    for offset in range(OFFS):
        first, second, third = offset // 9, offset // 3 % 3, offset % 3
        piece = windows[:, first : first + BRICK, second : second + BRICK, third : third + BRICK, :]
        pieces.append(piece.reshape(-1, windows.shape[-1]))
    return jnp.stack(pieces)


def local(features, occupancy, brick_pos, brick_count, weight, cotangent):
    slots = features.shape[2]
    chans = features.shape[-1]
    places = brick_pos[0, 0]
    alive = jnp.arange(slots, dtype=jnp.int32) < brick_count[0, 0]
    keeper = (occupancy[0, 0] * alive[:, None].astype(jnp.int32)).astype(jnp.bfloat16)
    keeper_rows = keeper.reshape(-1, 1).astype(jnp.float32)
    both = jnp.stack([features[0, 0], cotangent[0, 0]]) * keeper[None, :, :, None]
    grad_rows = both[1].reshape(-1, chans)
    dense = place_bricks(both, places, alive)
    padded = with_halo(dense)
    windows = cut_windows(padded, places)
    feat_stack = stack_offsets(windows[0])
    tiles = lax.axis_size("gx") * lax.axis_size("gy")
    weight_local = jnp.einsum("ve,dvc->dec", grad_rows, feat_stack, preferred_element_type=jnp.float32)
    weight_local = weight_local * jnp.float32(1.0 / tiles)
    half_done = butterfly_scatter(weight_local)
    output_sum = jnp.einsum("dvc,dce->ve", feat_stack, weight, preferred_element_type=jnp.float32)
    output_rows = (output_sum * keeper_rows).astype(jnp.bfloat16)
    grad_stack = stack_offsets(windows[1])
    input_sum = jnp.einsum("dvc,dec->ve", grad_stack, weight[::-1], preferred_element_type=jnp.float32)
    input_rows = (input_sum * keeper_rows).astype(jnp.bfloat16)
    half_done, output_rows, input_rows = lax.optimization_barrier((half_done, output_rows, input_rows))
    weight_total = butterfly_gather(half_done, weight_local)
    weight_grad = weight_total.transpose(0, 2, 1)
    output = output_rows.reshape(1, 1, slots, -1, chans)
    input_grad = input_rows.reshape(1, 1, slots, -1, chans)
    return (output, input_grad, weight_grad)


def solution(mesh):
    return jax.shard_map(
        local,
        mesh=mesh,
        in_specs=(
            P("gx", "gy", None, None, None),
            P("gx", "gy", None, None),
            P("gx", "gy", None),
            P("gx", "gy"),
            P(),
            P("gx", "gy", None, None, None),
        ),
        out_specs=(P("gx", "gy", None, None, None), P("gx", "gy", None, None, None), P()),
        check_vma=False,
    )
```

```python
import jax
import jax.numpy as jnp
from jax import lax
from jax.sharding import PartitionSpec as P

BRICK = 8
TBX = 2
TBY = 2
ZL = 4
OFFS = 27


def with_halo(value):
    nx, ny = value.shape[1], value.shape[2]
    size_x, size_y = lax.axis_size("gx"), lax.axis_size("gy")
    up_x = [(i, i + 1) for i in range(size_x - 1)]
    up_y = [(i, i + 1) for i in range(size_y - 1)]
    down_x = [(j, i) for i, j in up_x]
    down_y = [(j, i) for i, j in up_y]
    from_left = lax.ppermute(value[:, nx - 1 : nx], "gx", up_x)
    from_right = lax.ppermute(value[:, 0:1], "gx", down_x)

    def row(at):
        return jnp.concatenate([from_left[:, :, at], value[:, :, at], from_right[:, :, at]], 1)

    from_below = lax.ppermute(row(slice(ny - 1, ny)), "gy", up_y)
    from_above = lax.ppermute(row(slice(0, 1)), "gy", down_y)
    wide = jnp.concatenate([from_left, value, from_right], 1)
    full = jnp.concatenate([from_below, wide, from_above], 2)
    return jnp.pad(full, ((0, 0), (0, 0), (0, 0), (1, 1), (0, 0)))


FIRST = ("gx", 0)
ORDERS = (
    (("gy", 0), ("gx", 2), ("gy", 1), ("gx", 1), ("gx", 3), ("gy", 2), ("gy", 3)),
    (("gx", 2), ("gy", 1), ("gy", 0), ("gx", 3), ("gy", 2), ("gx", 1), ("gy", 3)),
)


def step_bit(step):
    axis, b = step
    return (lax.axis_index(axis) >> b) & 1


def step_pairs(k):
    sx, sy = lax.axis_size("gx"), lax.axis_size("gy")
    pairs = []
    for i in range(sx):
        for j in range(sy):
            axis, b = ORDERS[i & 1][k]
            pi, pj = (i ^ (1 << b), j) if axis == "gx" else (i, j ^ (1 << b))
            pairs.append((i * sy + j, pi * sy + pj))
    return pairs


def core_bit(k):
    return jnp.where(lax.axis_index("gx") & 1 == 0, step_bit(ORDERS[0][k]), step_bit(ORDERS[1][k]))


def butterfly_scatter(value):
    lanes = value.shape[-1]
    flat = value.reshape(-1, lanes)
    rows = flat.shape[0]
    parts = 1 << (1 + len(ORDERS[0]))
    padded_rows = -(-rows // parts) * parts
    buf = jnp.pad(flat, ((0, padded_rows - rows), (0, 0)))
    half = buf.shape[0] // 2
    bit = step_bit(FIRST)
    pairs = [(i, i ^ 1) for i in range(lax.axis_size("gx"))]
    keep = lax.dynamic_slice_in_dim(buf, bit * half, half, 0)
    send = lax.dynamic_slice_in_dim(buf, (1 - bit) * half, half, 0)
    buf = keep + lax.ppermute(send, "gx", pairs)
    for k in range(len(ORDERS[0])):
        half = buf.shape[0] // 2
        bit = core_bit(k)
        keep = lax.dynamic_slice_in_dim(buf, bit * half, half, 0)
        send = lax.dynamic_slice_in_dim(buf, (1 - bit) * half, half, 0)
        buf = keep + lax.ppermute(send, ("gx", "gy"), step_pairs(k))
    return buf


def join_halves(buf, got, bit):
    return jnp.concatenate([jnp.where(bit == 0, buf, got), jnp.where(bit == 0, got, buf)], 0)


def butterfly_gather(buf, like):
    for k in reversed(range(len(ORDERS[0]))):
        got = lax.ppermute(buf, ("gx", "gy"), step_pairs(k))
        buf = join_halves(buf, got, core_bit(k))
    got = lax.ppermute(buf, "gx", [(i, i ^ 1) for i in range(lax.axis_size("gx"))])
    buf = join_halves(buf, got, step_bit(FIRST))
    return buf[: like.size // like.shape[-1]].reshape(like.shape)


def place_bricks(bricks, places, alive):
    spots = jnp.arange(TBX * TBY * ZL, dtype=jnp.int32)
    picker = ((places[None, :] == spots[:, None]) & alive[None, :]).astype(jnp.bfloat16)
    dense = jnp.einsum("ps,tsvc->tpvc", picker, bricks, preferred_element_type=jnp.float32).astype(
        jnp.bfloat16
    )
    kinds, chans = bricks.shape[0], bricks.shape[-1]
    dense = dense.reshape(kinds, TBX, TBY, ZL, BRICK, BRICK, BRICK, chans)
    dense = dense.transpose(0, 1, 4, 2, 5, 3, 6, 7)
    return dense.reshape(kinds, TBX * BRICK, TBY * BRICK, ZL * BRICK, chans)


def cut_windows(padded, places):
    kinds, chans = padded.shape[0], padded.shape[-1]
    windows = []
    for slot in range(places.shape[0]):
        place = places[slot]
        starts = (0, place // (TBY * ZL) * BRICK, place // ZL % TBY * BRICK, place % ZL * BRICK, 0)
        windows.append(
            lax.dynamic_slice(padded, starts, (kinds, BRICK + 2, BRICK + 2, BRICK + 2, chans))
        )
    return jnp.stack(windows, 1)


def stack_offsets(windows):
    pieces = []
    for offset in range(OFFS):
        first, second, third = offset // 9, offset // 3 % 3, offset % 3
        piece = windows[:, first : first + BRICK, second : second + BRICK, third : third + BRICK, :]
        pieces.append(piece.reshape(-1, windows.shape[-1]))
    return jnp.stack(pieces)


def local(features, occupancy, brick_pos, brick_count, weight, cotangent):
    slots = features.shape[2]
    chans = features.shape[-1]
    places = brick_pos[0, 0]
    alive = jnp.arange(slots, dtype=jnp.int32) < brick_count[0, 0]
    keeper = (occupancy[0, 0] * alive[:, None].astype(jnp.int32)).astype(jnp.bfloat16)
    keeper_rows = keeper.reshape(-1, 1).astype(jnp.float32)
    both = jnp.stack([features[0, 0], cotangent[0, 0]]) * keeper[None, :, :, None]
    grad_rows = both[1].reshape(-1, chans)
    dense = place_bricks(both, places, alive)
    padded = with_halo(dense)
    windows = cut_windows(padded, places)
    feat_stack = stack_offsets(windows[0])
    tiles = lax.axis_size("gx") * lax.axis_size("gy")
    weight_local = jnp.einsum("ve,dvc->dec", grad_rows, feat_stack, preferred_element_type=jnp.float32)
    weight_local = weight_local * jnp.float32(1.0 / tiles)
    half_done = butterfly_scatter(weight_local)
    output_sum = jnp.einsum("dvc,dce->ve", feat_stack, weight, preferred_element_type=jnp.float32)
    output_rows = (output_sum * keeper_rows).astype(jnp.bfloat16)
    grad_stack = stack_offsets(windows[1])
    input_sum = jnp.einsum("dvc,dec->ve", grad_stack, weight[::-1], preferred_element_type=jnp.float32)
    input_rows = (input_sum * keeper_rows).astype(jnp.bfloat16)
    half_done, output_rows, input_rows = lax.optimization_barrier((half_done, output_rows, input_rows))
    weight_total = butterfly_gather(half_done, weight_local)
    weight_grad = weight_total.transpose(0, 2, 1)
    output = output_rows.reshape(1, 1, slots, -1, chans)
    input_grad = input_rows.reshape(1, 1, slots, -1, chans)
    return (output, input_grad, weight_grad)


def solution(mesh):
    return jax.shard_map(
        local,
        mesh=mesh,
        in_specs=(
            P("gx", "gy", None, None, None),
            P("gx", "gy", None, None),
            P("gx", "gy", None),
            P("gx", "gy"),
            P(),
            P("gx", "gy", None, None, None),
        ),
        out_specs=(P("gx", "gy", None, None, None), P("gx", "gy", None, None, None), P()),
        check_vma=False,
    )
```

```python
import jax
import jax.numpy as jnp
from jax import lax
from jax.sharding import PartitionSpec as P

BRICK = 8
TBX = 2
TBY = 2
ZL = 4
OFFS = 27


def with_halo(value):
    nx, ny = value.shape[1], value.shape[2]
    size_x, size_y = lax.axis_size("gx"), lax.axis_size("gy")
    up_x = [(i, i + 1) for i in range(size_x - 1)]
    up_y = [(i, i + 1) for i in range(size_y - 1)]
    down_x = [(j, i) for i, j in up_x]
    down_y = [(j, i) for i, j in up_y]
    from_left = lax.ppermute(value[:, nx - 1 : nx], "gx", up_x)
    from_right = lax.ppermute(value[:, 0:1], "gx", down_x)

    def row(at):
        return jnp.concatenate([from_left[:, :, at], value[:, :, at], from_right[:, :, at]], 1)

    from_below = lax.ppermute(row(slice(ny - 1, ny)), "gy", up_y)
    from_above = lax.ppermute(row(slice(0, 1)), "gy", down_y)
    return [tuple(part[kind : kind + 1] for part in (from_left, value, from_right, from_below, from_above))
            for kind in range(value.shape[0])]


def assemble(pieces):
    from_left, value, from_right, from_below, from_above = pieces
    wide = jnp.concatenate([from_left, value, from_right], 1)
    full = jnp.concatenate([from_below, wide, from_above], 2)
    return jnp.pad(full, ((0, 0), (0, 0), (0, 0), (1, 1), (0, 0)))


FIRST = ("gx", 0)
ORDERS = (
    (("gy", 0), ("gx", 2), ("gy", 1), ("gx", 1), ("gx", 3), ("gy", 2), ("gy", 3)),
    (("gx", 2), ("gy", 1), ("gy", 0), ("gx", 3), ("gy", 2), ("gx", 1), ("gy", 3)),
)


def step_bit(step):
    axis, b = step
    return (lax.axis_index(axis) >> b) & 1


def step_pairs(k):
    sx, sy = lax.axis_size("gx"), lax.axis_size("gy")
    pairs = []
    for i in range(sx):
        for j in range(sy):
            axis, b = ORDERS[i & 1][k]
            pi, pj = (i ^ (1 << b), j) if axis == "gx" else (i, j ^ (1 << b))
            pairs.append((i * sy + j, pi * sy + pj))
    return pairs


def core_bit(k):
    return jnp.where(lax.axis_index("gx") & 1 == 0, step_bit(ORDERS[0][k]), step_bit(ORDERS[1][k]))


def butterfly_scatter(value, extra):
    lanes = value.shape[-1]
    flat = value.reshape(-1, lanes)
    rows = flat.shape[0]
    parts = 1 << (1 + len(ORDERS[0]))
    padded_rows = -(-rows // parts) * parts
    buf = jnp.pad(flat, ((0, padded_rows - rows), (0, 0)))
    half = buf.shape[0] // 2
    bit = step_bit(FIRST)
    pairs = [(i, i ^ 1) for i in range(lax.axis_size("gx"))]
    keep = lax.dynamic_slice_in_dim(buf, bit * half, half, 0)
    send = lax.dynamic_slice_in_dim(buf, (1 - bit) * half, half, 0)
    buf = keep + lax.ppermute(send, "gx", pairs)
    buf, extra = lax.optimization_barrier((buf, extra))
    for k in range(len(ORDERS[0])):
        half = buf.shape[0] // 2
        bit = core_bit(k)
        keep = lax.dynamic_slice_in_dim(buf, bit * half, half, 0)
        send = lax.dynamic_slice_in_dim(buf, (1 - bit) * half, half, 0)
        buf = keep + lax.ppermute(send, ("gx", "gy"), step_pairs(k))
    return buf, extra


def join_halves(buf, got, bit):
    return jnp.concatenate([jnp.where(bit == 0, buf, got), jnp.where(bit == 0, got, buf)], 0)


def butterfly_gather(buf, like):
    for k in reversed(range(len(ORDERS[0]))):
        got = lax.ppermute(buf, ("gx", "gy"), step_pairs(k))
        buf = join_halves(buf, got, core_bit(k))
    got = lax.ppermute(buf, "gx", [(i, i ^ 1) for i in range(lax.axis_size("gx"))])
    buf = join_halves(buf, got, step_bit(FIRST))
    return buf[: like.size // like.shape[-1]].reshape(like.shape)


def place_bricks(bricks, places, alive):
    spots = jnp.arange(TBX * TBY * ZL, dtype=jnp.int32)
    picker = ((places[None, :] == spots[:, None]) & alive[None, :]).astype(jnp.bfloat16)
    dense = jnp.einsum("ps,tsvc->tpvc", picker, bricks, preferred_element_type=jnp.float32).astype(
        jnp.bfloat16
    )
    kinds, chans = bricks.shape[0], bricks.shape[-1]
    dense = dense.reshape(kinds, TBX, TBY, ZL, BRICK, BRICK, BRICK, chans)
    dense = dense.transpose(0, 1, 4, 2, 5, 3, 6, 7)
    return dense.reshape(kinds, TBX * BRICK, TBY * BRICK, ZL * BRICK, chans)


def cut_windows(padded, places):
    kinds, chans = padded.shape[0], padded.shape[-1]
    windows = []
    for slot in range(places.shape[0]):
        place = places[slot]
        starts = (0, place // (TBY * ZL) * BRICK, place // ZL % TBY * BRICK, place % ZL * BRICK, 0)
        windows.append(
            lax.dynamic_slice(padded, starts, (kinds, BRICK + 2, BRICK + 2, BRICK + 2, chans))
        )
    return jnp.stack(windows, 1)


def stack_offsets(windows):
    pieces = []
    for offset in range(OFFS):
        first, second, third = offset // 9, offset // 3 % 3, offset % 3
        piece = windows[:, first : first + BRICK, second : second + BRICK, third : third + BRICK, :]
        pieces.append(piece.reshape(-1, windows.shape[-1]))
    return jnp.stack(pieces)


def local(features, occupancy, brick_pos, brick_count, weight, cotangent):
    slots = features.shape[2]
    chans = features.shape[-1]
    places = brick_pos[0, 0]
    alive = jnp.arange(slots, dtype=jnp.int32) < brick_count[0, 0]
    keeper = (occupancy[0, 0] * alive[:, None].astype(jnp.int32)).astype(jnp.bfloat16)
    keeper_rows = keeper.reshape(-1, 1).astype(jnp.float32)
    both = jnp.stack([features[0, 0], cotangent[0, 0]]) * keeper[None, :, :, None]
    grad_rows = both[1].reshape(-1, chans)
    dense = place_bricks(both, places, alive)
    feat_pieces, grad_pieces = with_halo(dense)
    feat_stack = stack_offsets(cut_windows(assemble(feat_pieces), places)[0])
    tiles = lax.axis_size("gx") * lax.axis_size("gy")
    weight_local = jnp.einsum("ve,dvc->dec", grad_rows, feat_stack, preferred_element_type=jnp.float32)
    weight_local = weight_local * jnp.float32(1.0 / tiles)
    half_done, grad_pieces = butterfly_scatter(weight_local, grad_pieces)
    output_sum = jnp.einsum("dvc,dce->ve", feat_stack, weight, preferred_element_type=jnp.float32)
    output_rows = (output_sum * keeper_rows).astype(jnp.bfloat16)
    grad_stack = stack_offsets(cut_windows(assemble(grad_pieces), places)[0])
    input_sum = jnp.einsum("dvc,dec->ve", grad_stack, weight[::-1], preferred_element_type=jnp.float32)
    input_rows = (input_sum * keeper_rows).astype(jnp.bfloat16)
    half_done, output_rows, input_rows = lax.optimization_barrier((half_done, output_rows, input_rows))
    weight_total = butterfly_gather(half_done, weight_local)
    weight_grad = weight_total.transpose(0, 2, 1)
    output = output_rows.reshape(1, 1, slots, -1, chans)
    input_grad = input_rows.reshape(1, 1, slots, -1, chans)
    return (output, input_grad, weight_grad)


def solution(mesh):
    return jax.shard_map(
        local,
        mesh=mesh,
        in_specs=(
            P("gx", "gy", None, None, None),
            P("gx", "gy", None, None),
            P("gx", "gy", None),
            P("gx", "gy"),
            P(),
            P("gx", "gy", None, None, None),
        ),
        out_specs=(P("gx", "gy", None, None, None), P("gx", "gy", None, None, None), P()),
        check_vma=False,
    )
```

```python
import jax
import jax.numpy as jnp
from jax import lax
from jax.sharding import PartitionSpec as P

BRICK = 8
TBX = 2
TBY = 2
ZL = 4
OFFS = 27


def with_halo(value):
    nx, ny = value.shape[1], value.shape[2]
    size_x, size_y = lax.axis_size("gx"), lax.axis_size("gy")
    up_x = [(i, i + 1) for i in range(size_x - 1)]
    up_y = [(i, i + 1) for i in range(size_y - 1)]
    down_x = [(j, i) for i, j in up_x]
    down_y = [(j, i) for i, j in up_y]
    from_left = lax.ppermute(value[:, nx - 1 : nx], "gx", up_x)
    from_right = lax.ppermute(value[:, 0:1], "gx", down_x)

    def row(at):
        return jnp.concatenate([from_left[:, :, at], value[:, :, at], from_right[:, :, at]], 1)

    from_below = lax.ppermute(row(slice(ny - 1, ny)), "gy", up_y)
    from_above = lax.ppermute(row(slice(0, 1)), "gy", down_y)
    wide = jnp.concatenate([from_left, value, from_right], 1)
    full = jnp.concatenate([from_below, wide, from_above], 2)
    return full


FIRST = ("gx", 0)
ORDERS = (
    (("gy", 0), ("gx", 2), ("gy", 1), ("gx", 1), ("gx", 3), ("gy", 2), ("gy", 3)),
    (("gx", 2), ("gy", 1), ("gy", 0), ("gx", 3), ("gy", 2), ("gx", 1), ("gy", 3)),
)


def step_bit(step):
    axis, b = step
    return (lax.axis_index(axis) >> b) & 1


def step_pairs(k):
    sx, sy = lax.axis_size("gx"), lax.axis_size("gy")
    pairs = []
    for i in range(sx):
        for j in range(sy):
            axis, b = ORDERS[i & 1][k]
            pi, pj = (i ^ (1 << b), j) if axis == "gx" else (i, j ^ (1 << b))
            pairs.append((i * sy + j, pi * sy + pj))
    return pairs


def core_bit(k):
    return jnp.where(lax.axis_index("gx") & 1 == 0, step_bit(ORDERS[0][k]), step_bit(ORDERS[1][k]))


def butterfly_scatter(value):
    lanes = value.shape[-1]
    flat = value.reshape(-1, lanes)
    rows = flat.shape[0]
    parts = 1 << (1 + len(ORDERS[0]))
    padded_rows = -(-rows // parts) * parts
    buf = jnp.pad(flat, ((0, padded_rows - rows), (0, 0)))
    half = buf.shape[0] // 2
    bit = step_bit(FIRST)
    pairs = [(i, i ^ 1) for i in range(lax.axis_size("gx"))]
    keep = lax.dynamic_slice_in_dim(buf, bit * half, half, 0)
    send = lax.dynamic_slice_in_dim(buf, (1 - bit) * half, half, 0)
    buf = keep + lax.ppermute(send, "gx", pairs)
    for k in range(len(ORDERS[0])):
        half = buf.shape[0] // 2
        bit = core_bit(k)
        keep = lax.dynamic_slice_in_dim(buf, bit * half, half, 0)
        send = lax.dynamic_slice_in_dim(buf, (1 - bit) * half, half, 0)
        buf = keep + lax.ppermute(send, ("gx", "gy"), step_pairs(k))
    return buf


def join_halves(buf, got, bit):
    return jnp.concatenate([jnp.where(bit == 0, buf, got), jnp.where(bit == 0, got, buf)], 0)


def butterfly_gather(buf, like):
    for k in reversed(range(len(ORDERS[0]))):
        got = lax.ppermute(buf, ("gx", "gy"), step_pairs(k))
        buf = join_halves(buf, got, core_bit(k))
    got = lax.ppermute(buf, "gx", [(i, i ^ 1) for i in range(lax.axis_size("gx"))])
    buf = join_halves(buf, got, step_bit(FIRST))
    return buf[: like.size // like.shape[-1]].reshape(like.shape)


def place_bricks(bricks, places, alive):
    spots = jnp.arange(TBX * TBY * ZL, dtype=jnp.int32)
    picker = ((places[None, :] == spots[:, None]) & alive[None, :]).astype(jnp.bfloat16)
    dense = jnp.einsum("ps,tsvc->tpvc", picker, bricks, preferred_element_type=jnp.float32).astype(
        jnp.bfloat16
    )
    kinds, chans = bricks.shape[0], bricks.shape[-1]
    dense = dense.reshape(kinds, TBX, TBY, ZL, BRICK, BRICK, BRICK, chans)
    dense = dense.transpose(0, 1, 4, 2, 5, 3, 6, 7)
    return dense.reshape(kinds, TBX * BRICK, TBY * BRICK, ZL * BRICK, chans)


def cut_windows(padded, places):
    kinds, chans, depth = padded.shape[0], padded.shape[-1], padded.shape[3]
    windows = []
    for slot in range(places.shape[0]):
        place = places[slot]
        x0, y0, z0 = place // (TBY * ZL) * BRICK, place // ZL % TBY * BRICK, place % ZL * BRICK
        side = (kinds, BRICK + 2, BRICK + 2, 1, chans)
        main = lax.dynamic_slice(padded, (0, x0, y0, z0, 0), (kinds, BRICK + 2, BRICK + 2, BRICK, chans))
        below = lax.dynamic_slice(padded, (0, x0, y0, jnp.maximum(z0 - 1, 0), 0), side)
        above = lax.dynamic_slice(padded, (0, x0, y0, jnp.minimum(z0 + BRICK, depth - 1), 0), side)
        below = jnp.where(z0 > 0, below, jnp.zeros_like(below))
        above = jnp.where(z0 + BRICK < depth, above, jnp.zeros_like(above))
        windows.append(jnp.concatenate([below, main, above], 3))
    return jnp.stack(windows, 1)


def stack_offsets(windows):
    pieces = []
    for offset in range(OFFS):
        first, second, third = offset // 9, offset // 3 % 3, offset % 3
        piece = windows[:, first : first + BRICK, second : second + BRICK, third : third + BRICK, :]
        pieces.append(piece.reshape(-1, windows.shape[-1]))
    return jnp.stack(pieces)


def local(features, occupancy, brick_pos, brick_count, weight, cotangent):
    slots = features.shape[2]
    chans = features.shape[-1]
    places = brick_pos[0, 0]
    alive = jnp.arange(slots, dtype=jnp.int32) < brick_count[0, 0]
    keeper = (occupancy[0, 0] * alive[:, None].astype(jnp.int32)).astype(jnp.bfloat16)
    keeper_rows = keeper.reshape(-1, 1).astype(jnp.float32)
    both = jnp.stack([features[0, 0], cotangent[0, 0]]) * keeper[None, :, :, None]
    grad_rows = both[1].reshape(-1, chans)
    dense = place_bricks(both, places, alive)
    padded = with_halo(dense)
    windows = cut_windows(padded, places)
    feat_stack = stack_offsets(windows[0])
    tiles = lax.axis_size("gx") * lax.axis_size("gy")
    weight_local = jnp.einsum("ve,dvc->dec", grad_rows, feat_stack, preferred_element_type=jnp.float32)
    weight_local = weight_local * jnp.float32(1.0 / tiles)
    half_done = butterfly_scatter(weight_local)
    output_sum = jnp.einsum("dvc,dce->ve", feat_stack, weight, preferred_element_type=jnp.float32)
    output_rows = (output_sum * keeper_rows).astype(jnp.bfloat16)
    grad_stack = stack_offsets(windows[1])
    input_sum = jnp.einsum("dvc,dec->ve", grad_stack, weight[::-1], preferred_element_type=jnp.float32)
    input_rows = (input_sum * keeper_rows).astype(jnp.bfloat16)
    half_done, output_rows, input_rows = lax.optimization_barrier((half_done, output_rows, input_rows))
    weight_total = butterfly_gather(half_done, weight_local)
    weight_grad = weight_total.transpose(0, 2, 1)
    output = output_rows.reshape(1, 1, slots, -1, chans)
    input_grad = input_rows.reshape(1, 1, slots, -1, chans)
    return (output, input_grad, weight_grad)


def solution(mesh):
    return jax.shard_map(
        local,
        mesh=mesh,
        in_specs=(
            P("gx", "gy", None, None, None),
            P("gx", "gy", None, None),
            P("gx", "gy", None),
            P("gx", "gy"),
            P(),
            P("gx", "gy", None, None, None),
        ),
        out_specs=(P("gx", "gy", None, None, None), P("gx", "gy", None, None, None), P()),
        check_vma=False,
    )
```

```python
import jax
import jax.numpy as jnp
from jax import lax
from jax.sharding import PartitionSpec as P

BRICK = 8
TBX = 2
TBY = 2
ZL = 4
OFFS = 27


def with_halo(value):
    nx, ny = value.shape[1], value.shape[2]
    size_x, size_y = lax.axis_size("gx"), lax.axis_size("gy")
    up_x = [(i, i + 1) for i in range(size_x - 1)]
    up_y = [(i, i + 1) for i in range(size_y - 1)]
    down_x = [(j, i) for i, j in up_x]
    down_y = [(j, i) for i, j in up_y]
    from_left = lax.ppermute(value[:, nx - 1 : nx], "gx", up_x)
    from_right = lax.ppermute(value[:, 0:1], "gx", down_x)

    def row(at):
        return jnp.concatenate([from_left[:, :, at], value[:, :, at], from_right[:, :, at]], 1)

    from_below = lax.ppermute(row(slice(ny - 1, ny)), "gy", up_y)
    from_above = lax.ppermute(row(slice(0, 1)), "gy", down_y)
    wide = jnp.concatenate([from_left, value, from_right], 1)
    full = jnp.concatenate([from_below, wide, from_above], 2)
    return full


FIRST = ("gx", 0)
ORDERS = (
    (("gy", 0), ("gx", 2), ("gy", 1), ("gx", 1), ("gx", 3), ("gy", 2), ("gy", 3)),
    (("gx", 2), ("gy", 1), ("gy", 0), ("gx", 3), ("gy", 2), ("gx", 1), ("gy", 3)),
)


def step_bit(step):
    axis, b = step
    return (lax.axis_index(axis) >> b) & 1


def step_pairs(k):
    sx, sy = lax.axis_size("gx"), lax.axis_size("gy")
    pairs = []
    for i in range(sx):
        for j in range(sy):
            axis, b = ORDERS[i & 1][k]
            pi, pj = (i ^ (1 << b), j) if axis == "gx" else (i, j ^ (1 << b))
            pairs.append((i * sy + j, pi * sy + pj))
    return pairs


def core_bit(k):
    return jnp.where(lax.axis_index("gx") & 1 == 0, step_bit(ORDERS[0][k]), step_bit(ORDERS[1][k]))


def butterfly_scatter(value):
    lanes = value.shape[-1]
    flat = value.reshape(-1, lanes)
    rows = flat.shape[0]
    parts = 1 << (1 + len(ORDERS[0]))
    padded_rows = -(-rows // parts) * parts
    buf = jnp.pad(flat, ((0, padded_rows - rows), (0, 0)))
    half = buf.shape[0] // 2
    bit = step_bit(FIRST)
    pairs = [(i, i ^ 1) for i in range(lax.axis_size("gx"))]
    keep = lax.dynamic_slice_in_dim(buf, bit * half, half, 0)
    send = lax.dynamic_slice_in_dim(buf, (1 - bit) * half, half, 0)
    buf = keep + lax.ppermute(send, "gx", pairs)
    for k in range(len(ORDERS[0])):
        half = buf.shape[0] // 2
        bit = core_bit(k)
        keep = lax.dynamic_slice_in_dim(buf, bit * half, half, 0)
        send = lax.dynamic_slice_in_dim(buf, (1 - bit) * half, half, 0)
        buf = keep + lax.ppermute(send, ("gx", "gy"), step_pairs(k))
    return buf


def join_halves(buf, got, bit):
    return jnp.concatenate([jnp.where(bit == 0, buf, got), jnp.where(bit == 0, got, buf)], 0)


def butterfly_gather(buf, like):
    for k in reversed(range(len(ORDERS[0]))):
        got = lax.ppermute(buf, ("gx", "gy"), step_pairs(k))
        buf = join_halves(buf, got, core_bit(k))
    got = lax.ppermute(buf, "gx", [(i, i ^ 1) for i in range(lax.axis_size("gx"))])
    flip = (-1,) + like.shape[1:]
    mine = buf.reshape(flip).transpose(0, 2, 1)
    theirs = got.reshape(flip).transpose(0, 2, 1)
    return join_halves(mine, theirs, step_bit(FIRST))[: like.shape[0]]


def place_bricks(bricks, places, alive):
    spots = jnp.arange(TBX * TBY * ZL, dtype=jnp.int32)
    picker = ((places[None, :] == spots[:, None]) & alive[None, :]).astype(jnp.bfloat16)
    dense = jnp.einsum("ps,tsvc->tpvc", picker, bricks, preferred_element_type=jnp.float32).astype(
        jnp.bfloat16
    )
    kinds, chans = bricks.shape[0], bricks.shape[-1]
    dense = dense.reshape(kinds, TBX, TBY, ZL, BRICK, BRICK, BRICK, chans)
    dense = dense.transpose(0, 1, 4, 2, 5, 3, 6, 7)
    return dense.reshape(kinds, TBX * BRICK, TBY * BRICK, ZL * BRICK, chans)


def cut_windows(padded, places):
    kinds, chans, depth = padded.shape[0], padded.shape[-1], padded.shape[3]
    windows = []
    for slot in range(places.shape[0]):
        place = places[slot]
        x0, y0, z0 = place // (TBY * ZL) * BRICK, place // ZL % TBY * BRICK, place % ZL * BRICK
        side = (kinds, BRICK + 2, BRICK + 2, 1, chans)
        main = lax.dynamic_slice(padded, (0, x0, y0, z0, 0), (kinds, BRICK + 2, BRICK + 2, BRICK, chans))
        below = lax.dynamic_slice(padded, (0, x0, y0, jnp.maximum(z0 - 1, 0), 0), side)
        above = lax.dynamic_slice(padded, (0, x0, y0, jnp.minimum(z0 + BRICK, depth - 1), 0), side)
        below = jnp.where(z0 > 0, below, jnp.zeros_like(below))
        above = jnp.where(z0 + BRICK < depth, above, jnp.zeros_like(above))
        windows.append(jnp.concatenate([below, main, above], 3))
    return jnp.stack(windows, 1)


def stack_offsets(windows):
    pieces = []
    for offset in range(OFFS):
        first, second, third = offset // 9, offset // 3 % 3, offset % 3
        piece = windows[:, first : first + BRICK, second : second + BRICK, third : third + BRICK, :]
        pieces.append(piece.reshape(-1, windows.shape[-1]))
    return jnp.stack(pieces)


def local(features, occupancy, brick_pos, brick_count, weight, cotangent):
    slots = features.shape[2]
    chans = features.shape[-1]
    places = brick_pos[0, 0]
    alive = jnp.arange(slots, dtype=jnp.int32) < brick_count[0, 0]
    keeper = (occupancy[0, 0] * alive[:, None].astype(jnp.int32)).astype(jnp.bfloat16)
    keeper_rows = keeper.reshape(-1, 1).astype(jnp.float32)
    both = jnp.stack([features[0, 0], cotangent[0, 0]]) * keeper[None, :, :, None]
    grad_rows = both[1].reshape(-1, chans)
    dense = place_bricks(both, places, alive)
    padded = with_halo(dense)
    windows = cut_windows(padded, places)
    feat_stack = stack_offsets(windows[0])
    tiles = lax.axis_size("gx") * lax.axis_size("gy")
    weight_local = jnp.einsum("ve,dvc->dec", grad_rows, feat_stack, preferred_element_type=jnp.float32)
    weight_local = weight_local * jnp.float32(1.0 / tiles)
    half_done = butterfly_scatter(weight_local)
    output_sum = jnp.einsum("dvc,dce->ve", feat_stack, weight, preferred_element_type=jnp.float32)
    output_rows = (output_sum * keeper_rows).astype(jnp.bfloat16)
    grad_stack = stack_offsets(windows[1])
    input_sum = jnp.einsum("dvc,dec->ve", grad_stack, weight[::-1], preferred_element_type=jnp.float32)
    input_rows = (input_sum * keeper_rows).astype(jnp.bfloat16)
    half_done, output_rows, input_rows = lax.optimization_barrier((half_done, output_rows, input_rows))
    weight_total = butterfly_gather(half_done, weight_local)
    weight_grad = weight_total
    output = output_rows.reshape(1, 1, slots, -1, chans)
    input_grad = input_rows.reshape(1, 1, slots, -1, chans)
    return (output, input_grad, weight_grad)


def solution(mesh):
    return jax.shard_map(
        local,
        mesh=mesh,
        in_specs=(
            P("gx", "gy", None, None, None),
            P("gx", "gy", None, None),
            P("gx", "gy", None),
            P("gx", "gy"),
            P(),
            P("gx", "gy", None, None, None),
        ),
        out_specs=(P("gx", "gy", None, None, None), P("gx", "gy", None, None, None), P()),
        check_vma=False,
    )
```
